256 devices in a mesh: seq: 32 (over x, z), head: 8 (over y, core).
Axes of the slice: x: 4, y: 4, z: 8, core: 2. Of those that a mesh axis runs over, the one named last changes fastest.
Arguments:
- att_query: bfloat16 [8192, 16, 128], P('seq', 'head'), may hold values from -9 to 9
- att_key: bfloat16 [8192, 16, 128], P('seq', 'head'), may hold values from -9 to 9
- att_value: bfloat16 [8192, 16, 128], P('seq', 'head'), may hold values from -6 to 6
- norm_gain: float32 [16, 128], P('head'), may hold values from 0.1 to 1.9
- dn_query: bfloat16 [8192, 16, 128], P('seq', 'head'), may hold values from -6 to 6
- dn_key: bfloat16 [8192, 16, 128], P('seq', 'head'), may hold values from -4 to 4
- write_rate: float32 [8192, 16], P('seq', 'head'), may hold values from 0.04 to 0.9
- log_decay: float32 [8192, 16], P('seq', 'head'), may hold values from -1 to 0
- out_grad: bfloat16 [8192, 16, 128], P('seq', 'head'), may hold values from -6 to 6
Outputs:
- block_out: bfloat16 [8192, 16, 128], P('seq', 'head')
- att_query_grad: bfloat16 [8192, 16, 128], P('seq', 'head')
- att_key_grad: bfloat16 [8192, 16, 128], P('seq', 'head')
- att_value_grad: bfloat16 [8192, 16, 128], P('seq', 'head')
- gain_grad: float32 [16, 128], P('head')
- dn_query_grad: bfloat16 [8192, 16, 128], P('seq', 'head')
- dn_key_grad: bfloat16 [8192, 16, 128], P('seq', 'head')
- rate_grad: float32 [8192, 16], P('seq', 'head')
- decay_grad: float32 [8192, 16], P('seq', 'head')
The draws below stay inside these ranges and needn't reach their ends.
All inputs are finite; a program needn't handle non-finite values.
Results may differ from the reference program's by a relative error of at most 0.018.
Values may be sent and summed in bfloat16 or wider, within the bound.
No kernel may reach another device: no remote copies, remote signals or barrier semaphores. Data moves between devices by JAX's collectives and lax.ppermute only.
A program may use at most 64 MiB of HBM per device.

```python
import math
import jax
import jax.numpy as jnp
from jax import lax

TOK_DEV = 256
WIN = 1024
CH = 64
DH = 128
HEAD_TOTAL = 16
SEQUENCE_TOKENS = 8192


def base_field(key):
    return jnp.clip(jax.random.normal(key, (SEQUENCE_TOKENS, HEAD_TOTAL, DH), jnp.float32), -4.0, 4.0)


def draw_att_query(key, part):
    field = base_field(jax.random.fold_in(key, 21))
    return field.astype(jnp.bfloat16)


def draw_att_key(key, part):
    field = base_field(jax.random.fold_in(key, 22))
    return field.astype(jnp.bfloat16)


def draw_dn_key(key, part):
    key_pair = jax.random.split(jax.random.fold_in(key, 41), 2)
    shard_total = SEQUENCE_TOKENS // TOK_DEV
    chosen_count = max(4, DH // 8)
    scores = jax.random.randint(key_pair[0], (shard_total, HEAD_TOTAL, DH), 0, 1048576) * DH + jnp.arange(DH, dtype=jnp.int32)
    cutoff = lax.top_k(scores, chosen_count)[0][..., -1:]
    chosen = jnp.repeat(scores >= cutoff, TOK_DEV, axis=0)
    field = base_field(key_pair[1])
    return (field * jnp.where(chosen, 1.0, 0.03)).astype(jnp.bfloat16)


def draw_write_rate(key, part):
    key_pair = jax.random.split(jax.random.fold_in(key, 51), 2)
    head_base = jnp.exp(jax.random.uniform(key_pair[0], (HEAD_TOTAL,), jnp.float32, math.log(0.08), math.log(0.6)))
    jitter = jax.random.uniform(key_pair[1], (SEQUENCE_TOKENS, HEAD_TOTAL), jnp.float32, 0.5, 1.5)
    return jnp.minimum(head_base[None, :] * jitter, 0.9)


def draw_log_decay(key, part):
    split_random_keys = jax.random.split(jax.random.fold_in(key, 31), 7)
    quick_share = 0.5
    quick = jax.random.uniform(split_random_keys[0], (HEAD_TOTAL,), jnp.float32) < quick_share
    quick_rate = jax.random.uniform(split_random_keys[1], (HEAD_TOTAL,), jnp.float32, 1.0 / 50.0, 1.0 / 30.0)
    slow_rate = jax.random.uniform(split_random_keys[2], (HEAD_TOTAL,), jnp.float32, 0.1, 0.3) / SEQUENCE_TOKENS
    base_rate = jnp.where(quick, quick_rate, slow_rate)
    shard_factor = jnp.exp(jax.random.uniform(split_random_keys[3], (SEQUENCE_TOKENS // TOK_DEV, HEAD_TOTAL), jnp.float32, 0.0, 0.9))
    factor = jnp.repeat(shard_factor, TOK_DEV, axis=0)
    jitter = jax.random.uniform(split_random_keys[4], (SEQUENCE_TOKENS, HEAD_TOTAL), jnp.float32, 0.5, 1.5)
    spike_positions = jax.random.randint(split_random_keys[5], (1, HEAD_TOTAL, 3), 0, SEQUENCE_TOKENS)
    erased_values = jnp.any(jnp.arange(SEQUENCE_TOKENS)[:, None, None] == spike_positions, axis=2)
    drop = jnp.log(jax.random.uniform(split_random_keys[6], (SEQUENCE_TOKENS, HEAD_TOTAL), jnp.float32, 0.6, 0.85))
    return -base_rate[None, :] * factor * jitter + jnp.where(erased_values, drop, 0.0)


def shard_levels(rng, dims, cuts, low, top_value):
    def one(axis_at, blocks):
        steps = jax.random.uniform(jax.random.fold_in(jax.random.fold_in(rng, 6), axis_at), (blocks,), jnp.float32, low / len(cuts), top_value / len(cuts))
        return jnp.repeat(jnp.exp(steps), dims[axis_at] // blocks).reshape((-1,) + (1,) * (len(dims) - axis_at - 1))

    loudness = one(*cuts[0])
    for cut in cuts[1:]:
        loudness = loudness * one(*cut)
    return loudness


def gaussian(rng, extent, scale, bound, shards=(), kind=jnp.bfloat16):
    drawn = scale * jax.random.normal(rng, extent, jnp.float32)
    if shards:
        drawn = drawn * shard_levels(rng, extent, shards, -0.22, 0.18)
    return jnp.clip(drawn, -bound, bound).astype(kind)


def setup_inputs(seed: int = 0) -> dict:
    seeds = jax.random.split(jax.random.key(seed), 10)
    att_query = draw_att_query(jax.random.fold_in(seeds[9], 71), 0)
    att_key = draw_att_key(jax.random.fold_in(seeds[9], 71), 0)
    att_value = gaussian(seeds[2], (SEQUENCE_TOKENS, HEAD_TOTAL, DH), 1.0, 6.0, ((0, 32), (1, 8)))
    norm_gain = jnp.clip(1.0 + 0.18 * jax.random.normal(seeds[3], (HEAD_TOTAL, DH), jnp.float32), 0.1, 1.9)
    dn_query = gaussian(seeds[4], (SEQUENCE_TOKENS, HEAD_TOTAL, DH), 1.0, 6.0, ((0, 32), (1, 8)))
    dn_key = draw_dn_key(jax.random.fold_in(seeds[9], 71), 0)
    write_rate = draw_write_rate(jax.random.fold_in(seeds[9], 71), 0)
    log_decay = draw_log_decay(jax.random.fold_in(seeds[9], 71), 0)
    out_grad = gaussian(seeds[8], (SEQUENCE_TOKENS, HEAD_TOTAL, DH), 1.0, 6.0, ((0, 32), (1, 8)))
    return dict(att_query=att_query, att_key=att_key, att_value=att_value, norm_gain=norm_gain, dn_query=dn_query, dn_key=dn_key, write_rate=write_rate, log_decay=log_decay, out_grad=out_grad)


MATMUL_ACCURACY = lax.Precision.HIGHEST
EPSILON = 1e-06

def unit_rows(matrix):
    return matrix * lax.rsqrt(lax.optimization_barrier(jnp.sum(matrix * matrix, axis=-1, keepdims=True)) + EPSILON)

def delta_block(memory_state, pieces):
    query_vectors, key_vectors, value_rows, rate_rows, decay_rows = pieces
    length = key_vectors.shape[1]
    lower = jnp.tril(jnp.ones((length, length), jnp.float32))
    strict = lower - jnp.eye(length, dtype=jnp.float32)
    running_state = jnp.cumsum(decay_rows, axis=1)
    ratio = jnp.exp((running_state[:, :, None] - running_state[:, None, :]) * lower) * lower
    state_increment = jnp.exp(running_state)
    intersection = jnp.einsum('htk,hsk->hts', key_vectors, key_vectors, precision=MATMUL_ACCURACY)
    system = jnp.eye(length, dtype=jnp.float32) + rate_rows[:, :, None] * ratio * strict * intersection
    retrieved_values = jnp.einsum('nex,nxp->nep', key_vectors, memory_state, precision=MATMUL_ACCURACY)
    target = rate_rows[:, :, None] * (value_rows - state_increment[:, :, None] * retrieved_values)
    newest_state = jax.scipy.linalg.solve_triangular(system, target, lower=True, unit_diagonal=True)
    local_scores = jnp.einsum('htk,hsk->hts', query_vectors, key_vectors, precision=MATMUL_ACCURACY) * ratio
    state_output = state_increment[:, :, None] * jnp.einsum('nex,nxp->nep', query_vectors, memory_state, precision=MATMUL_ACCURACY)
    state_output = state_output + jnp.einsum('hts,hsv->htv', local_scores, newest_state, precision=MATMUL_ACCURACY)
    retained_state = jnp.exp(running_state[:, -1:] - running_state)
    memory_state = jnp.exp(running_state[:, -1])[:, None, None] * memory_state + jnp.einsum('wpa,wpn->wan', key_vectors * retained_state[:, :, None], newest_state, precision=MATMUL_ACCURACY)
    return (memory_state, state_output)

def delta_sweep(memory_state, query_vectors, key_vectors, value_rows, rate_rows, decay_rows):
    head_count, length = (key_vectors.shape[0], key_vectors.shape[1])
    blocks = length // CH

    def cut_blocks(array):
        return jnp.moveaxis(array.reshape((head_count, blocks, CH) + array.shape[2:]), 1, 0)
    last_state, state_output = lax.scan(delta_block, memory_state, (cut_blocks(query_vectors), cut_blocks(key_vectors), cut_blocks(value_rows), cut_blocks(rate_rows), cut_blocks(decay_rows)))
    return (last_state, jnp.moveaxis(state_output, 0, 1).reshape(head_count, length, state_output.shape[-1]))

def window_softmax(rows_here, keys_here, values_here, alive_keys):
    block_rows = rows_here.shape[0]
    span_rows = keys_here.shape[0]
    reach_back = span_rows - block_rows
    scores = jnp.einsum('qhd,khd->hqk', rows_here, keys_here) * rows_here.shape[-1] ** (-0.5)
    query_pos = jnp.arange(block_rows, dtype=jnp.int32)[:, None]
    key_pos = jnp.arange(span_rows, dtype=jnp.int32)[None, :]
    allowed = (key_pos > query_pos) & (key_pos <= query_pos + reach_back) & alive_keys[None, :]
    scores = jnp.where(allowed[None], scores, -1e+30)
    shifted = jnp.exp(scores - lax.optimization_barrier(jnp.max(scores, axis=-1, keepdims=True)))
    weights_bf = (shifted / lax.optimization_barrier(jnp.sum(shifted, axis=-1, keepdims=True))).astype(jnp.bfloat16)
    return jnp.einsum('hqk,khd->qhd', weights_bf.astype(jnp.float32), values_here)

def all_attention(query_vectors, key_vectors, value_rows):
    block_rows = min(512, TOK_DEV)
    padding = jnp.zeros((WIN,) + key_vectors.shape[1:], jnp.float32)
    padded_keys = jnp.concatenate([padding, key_vectors], axis=0)
    padded_values = jnp.concatenate([padding, value_rows], axis=0)

    def one_block(block_index):
        first_row = block_index * block_rows
        rows_here = lax.dynamic_slice_in_dim(query_vectors, first_row, block_rows, 0)
        keys_here = lax.dynamic_slice_in_dim(padded_keys, first_row, block_rows + WIN, 0)
        values_here = lax.dynamic_slice_in_dim(padded_values, first_row, block_rows + WIN, 0)
        alive_keys = first_row + jnp.arange(block_rows + WIN, dtype=jnp.int32) >= WIN
        return window_softmax(rows_here, keys_here, values_here, alive_keys)
    outputs = lax.map(jax.checkpoint(one_block), jnp.arange(SEQUENCE_TOKENS // block_rows, dtype=jnp.int32))
    return outputs.reshape(SEQUENCE_TOKENS, HEAD_TOTAL, DH)

def reference(att_query, att_key, att_value, norm_gain, dn_query, dn_key, write_rate, log_decay, out_grad):

    def forward(query_in, key_in, value_in, gain_in, dq_in, dk_in, rate_in, decay_in):
        attended = all_attention(query_in.astype(jnp.float32), key_in.astype(jnp.float32), value_in.astype(jnp.float32))
        inverse = lax.rsqrt(lax.optimization_barrier(jnp.mean(attended * attended, axis=(1, 2))) + EPSILON)
        values = (attended * inverse[:, None, None] * gain_in[None]).astype(jnp.bfloat16)
        start_state = jnp.zeros((HEAD_TOTAL, DH, DH), jnp.float32)
        unit_query = unit_rows(jnp.swapaxes(dq_in, 0, 1).astype(jnp.float32))
        unit_key = unit_rows(jnp.swapaxes(dk_in, 0, 1).astype(jnp.float32))
        last_state, state_output = delta_sweep(start_state, unit_query, unit_key, jnp.swapaxes(values, 0, 1).astype(jnp.float32), rate_in.T, decay_in.T)
        return jnp.swapaxes(state_output, 0, 1)
    state_output, pullback = jax.vjp(forward, att_query, att_key, att_value, norm_gain, dn_query, dn_key, write_rate, log_decay)
    grads = pullback(out_grad.astype(jnp.float32))
    return (state_output.astype(jnp.bfloat16), grads[0], grads[1], grads[2], grads[3], grads[4], grads[5], grads[6], grads[7])
```

```python
import jax
import jax.numpy as jnp
from jax import lax
from jax.sharding import PartitionSpec as P

WIN = 1024
CH = 64


MATMUL_ACCURACY = lax.Precision.HIGHEST
EPSILON = 1e-06


def shifted_2(block, axis, distance):
    devices = range(lax.axis_size(axis))
    route = [(i - distance, i) for i in devices if i - distance in devices]
    return lax.ppermute(block, axis, route)


def affine_scan(mat, vec, axis, direction):
    size = lax.axis_size(axis)
    distance = 1
    while distance < size:
        if 2 * distance >= size:
            came_vec = shifted_2(vec, axis, direction * distance)
            vec = apply_map(mat, came_vec) + vec
        else:
            came_mat, came_vec = shifted_2((mat, vec), axis, direction * distance)
            vec = apply_map(mat, came_vec) + vec
            mat = apply_map(mat, came_mat)
        distance *= 2
    return vec


def butterfly_sum(block, axis):
    size = lax.axis_size(axis)
    if size & (size - 1):
        return lax.psum(block, axis)
    distance = 1
    while distance < size:
        route = [(i, i ^ distance) for i in range(size)]
        block = block + lax.ppermute(block, axis, route)
        distance *= 2
    return block


def unit_rows(matrix):
    return matrix * lax.rsqrt(jnp.sum(matrix * matrix, axis=-1, keepdims=True) + EPSILON)


def delta_block(memory_state, pieces):
    query_vectors, key_vectors, value_rows, rate_rows, decay_rows = pieces
    length = key_vectors.shape[1]
    lower = jnp.tril(jnp.ones((length, length), jnp.float32))
    strict = lower - jnp.eye(length, dtype=jnp.float32)
    running_state = jnp.cumsum(decay_rows, axis=1)
    ratio = jnp.exp((running_state[:, :, None] - running_state[:, None, :]) * lower) * lower
    state_increment = jnp.exp(running_state)
    intersection = jnp.einsum("htk,hsk->hts", key_vectors, key_vectors, precision=MATMUL_ACCURACY)
    system = (
        jnp.eye(length, dtype=jnp.float32) + rate_rows[:, :, None] * ratio * strict * intersection
    )
    retrieved_values = jnp.einsum(
        "nex,nxp->nep", key_vectors, memory_state, precision=MATMUL_ACCURACY
    )
    target = rate_rows[:, :, None] * (value_rows - state_increment[:, :, None] * retrieved_values)
    newest_state = jax.scipy.linalg.solve_triangular(system, target, lower=True, unit_diagonal=True)
    local_scores = (
        jnp.einsum("htk,hsk->hts", query_vectors, key_vectors, precision=MATMUL_ACCURACY) * ratio
    )
    state_output = state_increment[:, :, None] * jnp.einsum(
        "nex,nxp->nep", query_vectors, memory_state, precision=MATMUL_ACCURACY
    )
    state_output = state_output + jnp.einsum(
        "hts,hsv->htv", local_scores, newest_state, precision=MATMUL_ACCURACY
    )
    retained_state = jnp.exp(running_state[:, -1:] - running_state)
    memory_state = jnp.exp(running_state[:, -1])[:, None, None] * memory_state + jnp.einsum(
        "wpa,wpn->wan",
        key_vectors * retained_state[:, :, None],
        newest_state,
        precision=MATMUL_ACCURACY,
    )
    return (memory_state, state_output)


def delta_sweep(memory_state, query_vectors, key_vectors, value_rows, rate_rows, decay_rows):
    head_count, length = (key_vectors.shape[0], key_vectors.shape[1])
    blocks = length // CH

    def cut_blocks(array):
        return jnp.moveaxis(array.reshape((head_count, blocks, CH) + array.shape[2:]), 1, 0)

    last_state, state_output = lax.scan(
        delta_block,
        memory_state,
        (
            cut_blocks(query_vectors),
            cut_blocks(key_vectors),
            cut_blocks(value_rows),
            cut_blocks(rate_rows),
            cut_blocks(decay_rows),
        ),
    )
    return (
        last_state,
        jnp.moveaxis(state_output, 0, 1).reshape(head_count, length, state_output.shape[-1]),
    )


def window_softmax(rows_here, keys_here, values_here, alive_keys):
    block_rows = rows_here.shape[0]
    span_rows = keys_here.shape[0]
    reach_back = span_rows - block_rows
    scores = jnp.einsum("qhd,khd->hqk", rows_here, keys_here) * rows_here.shape[-1] ** (-0.5)
    query_pos = jnp.arange(block_rows, dtype=jnp.int32)[:, None]
    key_pos = jnp.arange(span_rows, dtype=jnp.int32)[None, :]
    allowed = (key_pos > query_pos) & (key_pos <= query_pos + reach_back) & alive_keys[None, :]
    scores = jnp.where(allowed[None], scores, -1e30)
    shifted = jnp.exp(scores - jnp.max(scores, axis=-1, keepdims=True))
    weights_bf = (shifted / jnp.sum(shifted, axis=-1, keepdims=True)).astype(jnp.bfloat16)
    return jnp.einsum("hqk,khd->qhd", weights_bf.astype(jnp.float32), values_here)


def attend(query_vectors, key_vectors, value_rows, alive_keys):
    outputs = [window_softmax(query_vectors, key_vectors, value_rows, alive_keys)]
    return jnp.concatenate(outputs, axis=0)


def apply_map(matrix, operand):
    return jnp.einsum("hij,hjv->hiv", matrix, operand, precision=MATMUL_ACCURACY)


def body(
    att_query, att_key, att_value, norm_gain, dn_query, dn_key, write_rate, log_decay, out_grad
):
    row_count, head_count, head_width = att_query.shape
    rim_rows = min(WIN, row_count)
    reach_back = max(1, WIN // row_count)
    my_shard = lax.axis_index("seq")
    shard_count = lax.axis_size("seq")
    older_keys = []
    older_values = []
    for offset in range(reach_back):
        came_key, came_value = shifted_2((att_key, att_value), "seq", offset + 1)
        older_keys.insert(0, came_key)
        older_values.insert(0, came_value)
    all_keys = jnp.concatenate(older_keys + [att_key], axis=0).astype(jnp.float32)
    all_values = jnp.concatenate(older_values + [att_value], axis=0).astype(jnp.float32)
    alive_keys = my_shard * row_count - WIN + jnp.arange(WIN + row_count, dtype=jnp.int32) >= 0

    def attention_core(query_vectors, key_vectors, value_rows):
        return attend(query_vectors, key_vectors, value_rows, alive_keys)

    attended, attention_pull = jax.vjp(
        attention_core, att_query.astype(jnp.float32), all_keys, all_values
    )
    square_part = jnp.sum(attended * attended, axis=(1, 2))
    square_all = lax.psum(square_part, "head")
    features = head_count * lax.axis_size("head") * head_width
    inverse = lax.rsqrt(square_all / features + EPSILON)
    scaled = attended * inverse[:, None, None]
    values = (scaled * norm_gain[None]).astype(jnp.bfloat16)
    query_heads = jnp.swapaxes(dn_query, 0, 1).astype(jnp.float32)
    key_heads = jnp.swapaxes(dn_key, 0, 1).astype(jnp.float32)
    value_heads = jnp.swapaxes(values, 0, 1)
    rate_heads = write_rate.T
    decay_heads = log_decay.T
    identity = jnp.broadcast_to(
        jnp.eye(head_width, dtype=jnp.float32), (head_count, head_width, head_width)
    )
    seed_state = jnp.concatenate(
        [identity, jnp.zeros((head_count, head_width, head_width), jnp.float32)], axis=-1
    )
    folded_values = jnp.concatenate(
        [jnp.zeros(value_heads.shape, jnp.float32), value_heads.astype(jnp.float32)], axis=-1
    )
    summary, unused_out = delta_sweep(
        seed_state,
        unit_rows(query_heads),
        unit_rows(key_heads),
        folded_values,
        rate_heads,
        decay_heads,
    )
    carry_map = summary[..., :head_width]
    carry_add = summary[..., head_width:]
    empty_state = jnp.zeros_like(carry_add)

    start_state = shifted_2(affine_scan(carry_map, carry_add, "seq", 1), "seq", 1)

    def local_delta(start_in, query_in, key_in, value_in, rate_in, decay_in):
        last_state, state_output = delta_sweep(
            start_in,
            unit_rows(query_in),
            unit_rows(key_in),
            value_in.astype(jnp.float32),
            rate_in,
            decay_in,
        )
        return (state_output, last_state)

    (state_output, last_state), delta_pull = jax.vjp(
        local_delta, start_state, query_heads, key_heads, value_heads, rate_heads, decay_heads
    )
    cotangent = jnp.swapaxes(out_grad, 0, 1).astype(jnp.float32)
    start_weights = unused_out[..., :head_width]
    own_back = jnp.einsum("hti,htv->hiv", start_weights, cotangent, precision=MATMUL_ACCURACY)
    flipped = jnp.swapaxes(carry_map, 1, 2)
    later_grad = shifted_2(affine_scan(flipped, own_back, "seq", -1), "seq", -1)
    delta_grads = delta_pull((cotangent, later_grad))
    value_grad = jnp.swapaxes(delta_grads[3], 0, 1).astype(jnp.float32)
    weighted = value_grad * norm_gain[None]
    dot_part = jnp.sum(weighted * attended, axis=(1, 2))
    gain_part = jnp.sum(value_grad * scaled, axis=0)
    dot_all = lax.psum(dot_part, "head")
    gain_grad = butterfly_sum(gain_part, "seq")
    attended_grad = (
        inverse[:, None, None] * weighted
        - attended * (inverse * inverse * inverse * dot_all / features)[:, None, None]
    )
    query_grad, keys_grad, values_grad = attention_pull(attended_grad)
    own_key_grad = keys_grad[WIN:]
    own_value_grad = values_grad[WIN:]
    extra_key = jnp.zeros((rim_rows, head_count, head_width), jnp.float32)
    extra_value = jnp.zeros((rim_rows, head_count, head_width), jnp.float32)
    for offset in range(reach_back):
        segment = reach_back - 1 - offset
        sent_key = keys_grad[segment * rim_rows : (segment + 1) * rim_rows]
        sent_value = values_grad[segment * rim_rows : (segment + 1) * rim_rows]
        came_key, came_value = (
            shifted_2(sent_key.astype(jnp.bfloat16), "seq", -(offset + 1)).astype(sent_key.dtype),
            shifted_2(sent_value.astype(jnp.bfloat16), "seq", -(offset + 1)).astype(
                sent_value.dtype
            ),
        )
        extra_key = extra_key + came_key
        extra_value = extra_value + came_value
    own_key_grad = own_key_grad.at[row_count - rim_rows :].add(extra_key)
    own_value_grad = own_value_grad.at[row_count - rim_rows :].add(extra_value)
    block_out = jnp.swapaxes(state_output, 0, 1).astype(jnp.bfloat16)
    return (
        block_out,
        query_grad.astype(jnp.bfloat16),
        own_key_grad.astype(jnp.bfloat16),
        own_value_grad.astype(jnp.bfloat16),
        gain_grad,
        jnp.swapaxes(delta_grads[1], 0, 1).astype(jnp.bfloat16),
        jnp.swapaxes(delta_grads[2], 0, 1).astype(jnp.bfloat16),
        delta_grads[4].T,
        delta_grads[5].T,
    )


def solution(mesh):
    return jax.shard_map(
        body,
        mesh=mesh,
        in_specs=(
            P("seq", "head", None),
            P("seq", "head", None),
            P("seq", "head", None),
            P("head", None),
            P("seq", "head", None),
            P("seq", "head", None),
            P("seq", "head"),
            P("seq", "head"),
            P("seq", "head", None),
        ),
        out_specs=(
            P("seq", "head", None),
            P("seq", "head", None),
            P("seq", "head", None),
            P("seq", "head", None),
            P("head", None),
            P("seq", "head", None),
            P("seq", "head", None),
            P("seq", "head"),
            P("seq", "head"),
        ),
        check_vma=False,
    )
```

```python
import jax
import jax.numpy as jnp
from jax import lax
from jax.sharding import PartitionSpec as P

WIN = 1024
CH = 64


MATMUL_ACCURACY = lax.Precision.HIGHEST
EPSILON = 1e-06


def shifted_2(block, axis, distance):
    devices = range(lax.axis_size(axis))
    route = [(i - distance, i) for i in devices if i - distance in devices]
    return lax.ppermute(block, axis, route)


def affine_scan(mat, vec, axis, direction):
    size = lax.axis_size(axis)
    distance = 1
    while distance < size:
        if 2 * distance >= size:
            came_vec = shifted_2(vec, axis, direction * distance)
            vec = apply_map(mat, came_vec) + vec
        else:
            came_mat, came_vec = shifted_2((mat, vec), axis, direction * distance)
            vec = apply_map(mat, came_vec) + vec
            mat = apply_map(mat, came_mat)
        distance *= 2
    return vec


def butterfly_sum(block, axis):
    size = lax.axis_size(axis)
    if size & (size - 1):
        return lax.psum(block, axis)
    distance = 1
    while distance < size:
        route = [(i, i ^ distance) for i in range(size)]
        block = block + lax.ppermute(block, axis, route)
        distance *= 2
    return block


def unit_rows(matrix):
    return matrix * lax.rsqrt(jnp.sum(matrix * matrix, axis=-1, keepdims=True) + EPSILON)


def delta_block(memory_state, pieces):
    query_vectors, key_vectors, value_rows, rate_rows, decay_rows = pieces
    length = key_vectors.shape[1]
    lower = jnp.tril(jnp.ones((length, length), jnp.float32))
    strict = lower - jnp.eye(length, dtype=jnp.float32)
    running_state = jnp.cumsum(decay_rows, axis=1)
    ratio = jnp.exp((running_state[:, :, None] - running_state[:, None, :]) * lower) * lower
    state_increment = jnp.exp(running_state)
    intersection = jnp.einsum("htk,hsk->hts", key_vectors, key_vectors, precision=MATMUL_ACCURACY)
    system = (
        jnp.eye(length, dtype=jnp.float32) + rate_rows[:, :, None] * ratio * strict * intersection
    )
    retrieved_values = jnp.einsum(
        "nex,nxp->nep", key_vectors, memory_state, precision=MATMUL_ACCURACY
    )
    target = rate_rows[:, :, None] * (value_rows - state_increment[:, :, None] * retrieved_values)
    newest_state = jax.scipy.linalg.solve_triangular(system, target, lower=True, unit_diagonal=True)
    local_scores = (
        jnp.einsum("htk,hsk->hts", query_vectors, key_vectors, precision=MATMUL_ACCURACY) * ratio
    )
    state_output = state_increment[:, :, None] * jnp.einsum(
        "nex,nxp->nep", query_vectors, memory_state, precision=MATMUL_ACCURACY
    )
    state_output = state_output + jnp.einsum(
        "hts,hsv->htv", local_scores, newest_state, precision=MATMUL_ACCURACY
    )
    retained_state = jnp.exp(running_state[:, -1:] - running_state)
    memory_state = jnp.exp(running_state[:, -1])[:, None, None] * memory_state + jnp.einsum(
        "wpa,wpn->wan",
        key_vectors * retained_state[:, :, None],
        newest_state,
        precision=MATMUL_ACCURACY,
    )
    return (memory_state, state_output)


def delta_sweep(memory_state, query_vectors, key_vectors, value_rows, rate_rows, decay_rows):
    head_count, length = (key_vectors.shape[0], key_vectors.shape[1])
    blocks = length // CH

    def cut_blocks(array):
        return jnp.moveaxis(array.reshape((head_count, blocks, CH) + array.shape[2:]), 1, 0)

    last_state, state_output = lax.scan(
        delta_block,
        memory_state,
        (
            cut_blocks(query_vectors),
            cut_blocks(key_vectors),
            cut_blocks(value_rows),
            cut_blocks(rate_rows),
            cut_blocks(decay_rows),
        ),
    )
    return (
        last_state,
        jnp.moveaxis(state_output, 0, 1).reshape(head_count, length, state_output.shape[-1]),
    )


def block_prep(query_heads, key_heads, value_heads, rate_heads, decay_heads):
    head_count, length, width = key_heads.shape
    blocks = length // CH

    def cut(array):
        return array.reshape((head_count, blocks, CH) + array.shape[2:])

    query_vectors = cut(unit_rows(query_heads))
    key_vectors = cut(unit_rows(key_heads))
    value_rows = cut(value_heads.astype(jnp.float32))
    rate_rows = cut(rate_heads)
    running_state = jnp.cumsum(cut(decay_heads), axis=-1)
    lower = jnp.tril(jnp.ones((CH, CH), jnp.float32))
    strict = lower - jnp.eye(CH, dtype=jnp.float32)
    ratio = jnp.exp((running_state[..., :, None] - running_state[..., None, :]) * lower) * lower
    state_increment = jnp.exp(running_state)
    intersection = jnp.einsum(
        "hbtk,hbsk->hbts", key_vectors, key_vectors, precision=MATMUL_ACCURACY
    )
    system = jnp.eye(CH, dtype=jnp.float32) + rate_rows[..., None] * ratio * strict * intersection
    sides = jnp.concatenate(
        [
            rate_rows[..., None] * value_rows,
            (rate_rows * state_increment)[..., None] * key_vectors,
        ],
        axis=-1,
    )
    solved = jax.scipy.linalg.solve_triangular(system, sides, lower=True, unit_diagonal=True)
    fresh = solved[..., : value_rows.shape[-1]]
    pulled = solved[..., value_rows.shape[-1] :]
    local_scores = (
        jnp.einsum("hbtk,hbsk->hbts", query_vectors, key_vectors, precision=MATMUL_ACCURACY)
        * ratio
    )
    base_out = jnp.einsum("hbts,hbsv->hbtv", local_scores, fresh, precision=MATMUL_ACCURACY)
    read_map = state_increment[..., None] * query_vectors - jnp.einsum(
        "hbts,hbsk->hbtk", local_scores, pulled, precision=MATMUL_ACCURACY
    )
    retained = key_vectors * jnp.exp(running_state[..., -1:] - running_state)[..., None]
    step_map = jnp.exp(running_state[..., -1])[..., None, None] * jnp.eye(
        width, dtype=jnp.float32
    ) - jnp.einsum("hbtk,hbtj->hbkj", retained, pulled, precision=MATMUL_ACCURACY)
    step_add = jnp.einsum("hbtk,hbtv->hbkv", retained, fresh, precision=MATMUL_ACCURACY)
    return (step_map, step_add, base_out, read_map)


def summarize(step_map, step_add):
    carry_map = step_map[:, 0]
    carry_add = step_add[:, 0]
    for block in range(1, step_map.shape[1]):
        carry_add = apply_map(step_map[:, block], carry_add) + step_add[:, block]
        carry_map = apply_map(step_map[:, block], carry_map)
    return (carry_map, carry_add)


def local_chain(start_state, step_map, step_add, base_out, read_map):
    state = start_state
    outputs = []
    for block in range(step_map.shape[1]):
        outputs.append(base_out[:, block] + apply_map(read_map[:, block], state))
        state = apply_map(step_map[:, block], state) + step_add[:, block]
    return (jnp.concatenate(outputs, axis=1), state)


def window_softmax(rows_here, keys_here, values_here, alive_keys):
    block_rows = rows_here.shape[0]
    span_rows = keys_here.shape[0]
    reach_back = span_rows - block_rows
    scores = jnp.einsum("qhd,khd->hqk", rows_here, keys_here) * rows_here.shape[-1] ** (-0.5)
    query_pos = jnp.arange(block_rows, dtype=jnp.int32)[:, None]
    key_pos = jnp.arange(span_rows, dtype=jnp.int32)[None, :]
    allowed = (key_pos > query_pos) & (key_pos <= query_pos + reach_back) & alive_keys[None, :]
    scores = jnp.where(allowed[None], scores, -1e30)
    shifted = jnp.exp(scores - jnp.max(scores, axis=-1, keepdims=True))
    weights_bf = (shifted / jnp.sum(shifted, axis=-1, keepdims=True)).astype(jnp.bfloat16)
    return jnp.einsum("hqk,khd->qhd", weights_bf.astype(jnp.float32), values_here)


def attend(query_vectors, key_vectors, value_rows, alive_keys):
    outputs = [window_softmax(query_vectors, key_vectors, value_rows, alive_keys)]
    return jnp.concatenate(outputs, axis=0)


def apply_map(matrix, operand):
    return jnp.einsum("hij,hjv->hiv", matrix, operand, precision=MATMUL_ACCURACY)


def body(
    att_query, att_key, att_value, norm_gain, dn_query, dn_key, write_rate, log_decay, out_grad
):
    row_count, head_count, head_width = att_query.shape
    rim_rows = min(WIN, row_count)
    reach_back = max(1, WIN // row_count)
    my_shard = lax.axis_index("seq")
    shard_count = lax.axis_size("seq")
    older_keys = []
    older_values = []
    for offset in range(reach_back):
        came_key, came_value = shifted_2((att_key, att_value), "seq", offset + 1)
        older_keys.insert(0, came_key)
        older_values.insert(0, came_value)
    all_keys = jnp.concatenate(older_keys + [att_key], axis=0).astype(jnp.float32)
    all_values = jnp.concatenate(older_values + [att_value], axis=0).astype(jnp.float32)
    alive_keys = my_shard * row_count - WIN + jnp.arange(WIN + row_count, dtype=jnp.int32) >= 0

    def attention_core(query_vectors, key_vectors, value_rows):
        return attend(query_vectors, key_vectors, value_rows, alive_keys)

    attended, attention_pull = jax.vjp(
        attention_core, att_query.astype(jnp.float32), all_keys, all_values
    )
    square_part = jnp.sum(attended * attended, axis=(1, 2))
    square_all = lax.psum(square_part, "head")
    features = head_count * lax.axis_size("head") * head_width
    inverse = lax.rsqrt(square_all / features + EPSILON)
    scaled = attended * inverse[:, None, None]
    values = (scaled * norm_gain[None]).astype(jnp.bfloat16)
    query_heads = jnp.swapaxes(dn_query, 0, 1).astype(jnp.float32)
    key_heads = jnp.swapaxes(dn_key, 0, 1).astype(jnp.float32)
    value_heads = jnp.swapaxes(values, 0, 1)
    rate_heads = write_rate.T
    decay_heads = log_decay.T
    prep_out, prep_pull = jax.vjp(
        block_prep, query_heads, key_heads, value_heads, rate_heads, decay_heads
    )
    carry_map, carry_add = summarize(prep_out[0], prep_out[1])
    empty_state = jnp.zeros_like(carry_add)
    start_state = shifted_2(affine_scan(carry_map, carry_add, "seq", 1), "seq", 1)
    (state_output, last_state), chain_pull = jax.vjp(local_chain, start_state, *prep_out)
    cotangent = jnp.swapaxes(out_grad, 0, 1).astype(jnp.float32)
    own_back = chain_pull((cotangent, empty_state))[0]
    flipped = jnp.swapaxes(carry_map, 1, 2)
    later_grad = shifted_2(affine_scan(flipped, own_back, "seq", -1), "seq", -1)
    chain_grads = chain_pull((cotangent, later_grad))
    delta_grads = (None,) + prep_pull(tuple(chain_grads[1:]))
    value_grad = jnp.swapaxes(delta_grads[3], 0, 1).astype(jnp.float32)
    weighted = value_grad * norm_gain[None]
    dot_part = jnp.sum(weighted * attended, axis=(1, 2))
    gain_part = jnp.sum(value_grad * scaled, axis=0)
    dot_all = lax.psum(dot_part, "head")
    gain_grad = butterfly_sum(gain_part, "seq")
    attended_grad = (
        inverse[:, None, None] * weighted
        - attended * (inverse * inverse * inverse * dot_all / features)[:, None, None]
    )
    query_grad, keys_grad, values_grad = attention_pull(attended_grad)
    own_key_grad = keys_grad[WIN:]
    own_value_grad = values_grad[WIN:]
    extra_key = jnp.zeros((rim_rows, head_count, head_width), jnp.float32)
    extra_value = jnp.zeros((rim_rows, head_count, head_width), jnp.float32)
    for offset in range(reach_back):
        segment = reach_back - 1 - offset
        sent_key = keys_grad[segment * rim_rows : (segment + 1) * rim_rows]
        sent_value = values_grad[segment * rim_rows : (segment + 1) * rim_rows]
        came_key, came_value = (
            shifted_2(sent_key.astype(jnp.bfloat16), "seq", -(offset + 1)).astype(sent_key.dtype),
            shifted_2(sent_value.astype(jnp.bfloat16), "seq", -(offset + 1)).astype(
                sent_value.dtype
            ),
        )
        extra_key = extra_key + came_key
        extra_value = extra_value + came_value
    own_key_grad = own_key_grad.at[row_count - rim_rows :].add(extra_key)
    own_value_grad = own_value_grad.at[row_count - rim_rows :].add(extra_value)
    block_out = jnp.swapaxes(state_output, 0, 1).astype(jnp.bfloat16)
    return (
        block_out,
        query_grad.astype(jnp.bfloat16),
        own_key_grad.astype(jnp.bfloat16),
        own_value_grad.astype(jnp.bfloat16),
        gain_grad,
        jnp.swapaxes(delta_grads[1], 0, 1).astype(jnp.bfloat16),
        jnp.swapaxes(delta_grads[2], 0, 1).astype(jnp.bfloat16),
        delta_grads[4].T,
        delta_grads[5].T,
    )


def solution(mesh):
    return jax.shard_map(
        body,
        mesh=mesh,
        in_specs=(
            P("seq", "head", None),
            P("seq", "head", None),
            P("seq", "head", None),
            P("head", None),
            P("seq", "head", None),
            P("seq", "head", None),
            P("seq", "head"),
            P("seq", "head"),
            P("seq", "head", None),
        ),
        out_specs=(
            P("seq", "head", None),
            P("seq", "head", None),
            P("seq", "head", None),
            P("seq", "head", None),
            P("head", None),
            P("seq", "head", None),
            P("seq", "head", None),
            P("seq", "head"),
            P("seq", "head"),
        ),
        check_vma=False,
    )
```

```python
import jax
import jax.numpy as jnp
from jax import lax
from jax.sharding import PartitionSpec as P

WIN = 1024
CH = 64


MATMUL_ACCURACY = lax.Precision.HIGHEST
EPSILON = 1e-06


def shifted_2(block, axis, distance):
    devices = range(lax.axis_size(axis))
    route = [(i - distance, i) for i in devices if i - distance in devices]
    return lax.ppermute(block, axis, route)


def affine_scan(mat, vec, axis, direction):
    size = lax.axis_size(axis)
    distance = 1
    while distance < size:
        if 2 * distance >= size:
            came_vec = shifted_2(vec, axis, direction * distance)
            vec = apply_map(mat, came_vec) + vec
        else:
            came_mat, came_vec = shifted_2((mat, vec), axis, direction * distance)
            vec = apply_map(mat, came_vec) + vec
            mat = apply_map(mat, came_mat)
        distance *= 2
    return vec


def butterfly_sum(block, axis):
    size = lax.axis_size(axis)
    if size & (size - 1):
        return lax.psum(block, axis)
    distance = 1
    while distance < size:
        route = [(i, i ^ distance) for i in range(size)]
        block = block + lax.ppermute(block, axis, route)
        distance *= 2
    return block


def unit_rows(matrix):
    return matrix * lax.rsqrt(jnp.sum(matrix * matrix, axis=-1, keepdims=True) + EPSILON)


def delta_block(memory_state, pieces):
    query_vectors, key_vectors, value_rows, rate_rows, decay_rows = pieces
    length = key_vectors.shape[1]
    lower = jnp.tril(jnp.ones((length, length), jnp.float32))
    strict = lower - jnp.eye(length, dtype=jnp.float32)
    running_state = jnp.cumsum(decay_rows, axis=1)
    ratio = jnp.exp((running_state[:, :, None] - running_state[:, None, :]) * lower) * lower
    state_increment = jnp.exp(running_state)
    intersection = jnp.einsum("htk,hsk->hts", key_vectors, key_vectors, precision=MATMUL_ACCURACY)
    system = (
        jnp.eye(length, dtype=jnp.float32) + rate_rows[:, :, None] * ratio * strict * intersection
    )
    retrieved_values = jnp.einsum(
        "nex,nxp->nep", key_vectors, memory_state, precision=MATMUL_ACCURACY
    )
    target = rate_rows[:, :, None] * (value_rows - state_increment[:, :, None] * retrieved_values)
    newest_state = jax.scipy.linalg.solve_triangular(system, target, lower=True, unit_diagonal=True)
    local_scores = (
        jnp.einsum("htk,hsk->hts", query_vectors, key_vectors, precision=MATMUL_ACCURACY) * ratio
    )
    state_output = state_increment[:, :, None] * jnp.einsum(
        "nex,nxp->nep", query_vectors, memory_state, precision=MATMUL_ACCURACY
    )
    state_output = state_output + jnp.einsum(
        "hts,hsv->htv", local_scores, newest_state, precision=MATMUL_ACCURACY
    )
    retained_state = jnp.exp(running_state[:, -1:] - running_state)
    memory_state = jnp.exp(running_state[:, -1])[:, None, None] * memory_state + jnp.einsum(
        "wpa,wpn->wan",
        key_vectors * retained_state[:, :, None],
        newest_state,
        precision=MATMUL_ACCURACY,
    )
    return (memory_state, state_output)


def delta_sweep(memory_state, query_vectors, key_vectors, value_rows, rate_rows, decay_rows):
    head_count, length = (key_vectors.shape[0], key_vectors.shape[1])
    blocks = length // CH

    def cut_blocks(array):
        return jnp.moveaxis(array.reshape((head_count, blocks, CH) + array.shape[2:]), 1, 0)

    last_state, state_output = lax.scan(
        delta_block,
        memory_state,
        (
            cut_blocks(query_vectors),
            cut_blocks(key_vectors),
            cut_blocks(value_rows),
            cut_blocks(rate_rows),
            cut_blocks(decay_rows),
        ),
    )
    return (
        last_state,
        jnp.moveaxis(state_output, 0, 1).reshape(head_count, length, state_output.shape[-1]),
    )


def block_prep(query_heads, key_heads, value_heads, rate_heads, decay_heads):
    head_count, length, width = key_heads.shape
    blocks = length // CH

    def cut(array):
        return array.reshape((head_count, blocks, CH) + array.shape[2:])

    query_vectors = cut(unit_rows(query_heads))
    key_vectors = cut(unit_rows(key_heads))
    value_rows = cut(value_heads.astype(jnp.float32))
    rate_rows = cut(rate_heads)
    running_state = jnp.cumsum(cut(decay_heads), axis=-1)
    lower = jnp.tril(jnp.ones((CH, CH), jnp.float32))
    strict = lower - jnp.eye(CH, dtype=jnp.float32)
    ratio = jnp.exp((running_state[..., :, None] - running_state[..., None, :]) * lower) * lower
    state_increment = jnp.exp(running_state)
    intersection = jnp.einsum(
        "hbtk,hbsk->hbts", key_vectors, key_vectors, precision=MATMUL_ACCURACY
    )
    system = jnp.eye(CH, dtype=jnp.float32) + rate_rows[..., None] * ratio * strict * intersection
    sides = jnp.concatenate(
        [
            rate_rows[..., None] * value_rows,
            (rate_rows * state_increment)[..., None] * key_vectors,
        ],
        axis=-1,
    )
    solved = jax.scipy.linalg.solve_triangular(system, sides, lower=True, unit_diagonal=True)
    fresh = solved[..., : value_rows.shape[-1]]
    pulled = solved[..., value_rows.shape[-1] :]
    local_scores = (
        jnp.einsum("hbtk,hbsk->hbts", query_vectors, key_vectors, precision=MATMUL_ACCURACY)
        * ratio
    )
    base_out = jnp.einsum("hbts,hbsv->hbtv", local_scores, fresh, precision=MATMUL_ACCURACY)
    read_map = state_increment[..., None] * query_vectors - jnp.einsum(
        "hbts,hbsk->hbtk", local_scores, pulled, precision=MATMUL_ACCURACY
    )
    retained = key_vectors * jnp.exp(running_state[..., -1:] - running_state)[..., None]
    step_map = jnp.exp(running_state[..., -1])[..., None, None] * jnp.eye(
        width, dtype=jnp.float32
    ) - jnp.einsum("hbtk,hbtj->hbkj", retained, pulled, precision=MATMUL_ACCURACY)
    step_add = jnp.einsum("hbtk,hbtv->hbkv", retained, fresh, precision=MATMUL_ACCURACY)
    return (step_map, step_add, base_out, read_map)


def summarize(step_map, step_add):
    carry_map = step_map[:, 0]
    carry_add = step_add[:, 0]
    for block in range(1, step_map.shape[1]):
        carry_add = apply_map(step_map[:, block], carry_add) + step_add[:, block]
        carry_map = apply_map(step_map[:, block], carry_map)
    return (carry_map, carry_add)


def local_chain(start_state, step_map, step_add, base_out, read_map):
    state = start_state
    outputs = []
    for block in range(step_map.shape[1]):
        outputs.append(base_out[:, block] + apply_map(read_map[:, block], state))
        state = apply_map(step_map[:, block], state) + step_add[:, block]
    return (jnp.concatenate(outputs, axis=1), state)


def back_chain(step_map, read_map, cotangent):
    blocks = step_map.shape[1]
    pieces = cotangent.reshape((cotangent.shape[0], blocks, CH) + cotangent.shape[2:])
    start_grad = None
    for block in reversed(range(blocks)):
        term = jnp.einsum(
            "htk,htv->hkv", read_map[:, block], pieces[:, block], precision=MATMUL_ACCURACY
        )
        if start_grad is not None:
            term = term + apply_map(jnp.swapaxes(step_map[:, block], 1, 2), start_grad)
        start_grad = term
    return start_grad


def window_softmax(rows_here, keys_here, values_here, alive_keys):
    block_rows = rows_here.shape[0]
    span_rows = keys_here.shape[0]
    reach_back = span_rows - block_rows
    scores = jnp.einsum("qhd,khd->hqk", rows_here, keys_here) * rows_here.shape[-1] ** (-0.5)
    query_pos = jnp.arange(block_rows, dtype=jnp.int32)[:, None]
    key_pos = jnp.arange(span_rows, dtype=jnp.int32)[None, :]
    allowed = (key_pos > query_pos) & (key_pos <= query_pos + reach_back) & alive_keys[None, :]
    scores = jnp.where(allowed[None], scores, -1e30)
    shifted = jnp.exp(scores - jnp.max(scores, axis=-1, keepdims=True))
    weights_bf = (shifted / jnp.sum(shifted, axis=-1, keepdims=True)).astype(jnp.bfloat16)
    return jnp.einsum("hqk,khd->qhd", weights_bf.astype(jnp.float32), values_here)


def attend(query_vectors, key_vectors, value_rows, alive_keys):
    outputs = [window_softmax(query_vectors, key_vectors, value_rows, alive_keys)]
    return jnp.concatenate(outputs, axis=0)


def apply_map(matrix, operand):
    return jnp.einsum("hij,hjv->hiv", matrix, operand, precision=MATMUL_ACCURACY)


def body(
    att_query, att_key, att_value, norm_gain, dn_query, dn_key, write_rate, log_decay, out_grad
):
    row_count, head_count, head_width = att_query.shape
    rim_rows = min(WIN, row_count)
    reach_back = max(1, WIN // row_count)
    my_shard = lax.axis_index("seq")
    shard_count = lax.axis_size("seq")
    older_keys = []
    older_values = []
    key_value = jnp.concatenate([att_key, att_value], axis=-1)
    for offset in range(reach_back):
        came = shifted_2(key_value, "seq", offset + 1)
        older_keys.insert(0, came[..., :head_width])
        older_values.insert(0, came[..., head_width:])
    all_keys = jnp.concatenate(older_keys + [att_key], axis=0).astype(jnp.float32)
    all_values = jnp.concatenate(older_values + [att_value], axis=0).astype(jnp.float32)
    alive_keys = my_shard * row_count - WIN + jnp.arange(WIN + row_count, dtype=jnp.int32) >= 0

    def attention_core(query_vectors, key_vectors, value_rows):
        return attend(query_vectors, key_vectors, value_rows, alive_keys)

    attended, attention_pull = jax.vjp(
        attention_core, att_query.astype(jnp.float32), all_keys, all_values
    )
    square_part = jnp.sum(attended * attended, axis=(1, 2))
    square_all = lax.psum(square_part, "head")
    features = head_count * lax.axis_size("head") * head_width
    inverse = lax.rsqrt(square_all / features + EPSILON)
    scaled = attended * inverse[:, None, None]
    values = (scaled * norm_gain[None]).astype(jnp.bfloat16)
    query_heads = jnp.swapaxes(dn_query, 0, 1).astype(jnp.float32)
    key_heads = jnp.swapaxes(dn_key, 0, 1).astype(jnp.float32)
    value_heads = jnp.swapaxes(values, 0, 1)
    rate_heads = write_rate.T
    decay_heads = log_decay.T
    prep_out, prep_pull = jax.vjp(
        block_prep, query_heads, key_heads, value_heads, rate_heads, decay_heads
    )
    carry_map, carry_add = summarize(prep_out[0], prep_out[1])
    empty_state = jnp.zeros_like(carry_add)
    start_state = shifted_2(affine_scan(carry_map, carry_add, "seq", 1), "seq", 1)
    (state_output, last_state), chain_pull = jax.vjp(local_chain, start_state, *prep_out)
    cotangent = jnp.swapaxes(out_grad, 0, 1).astype(jnp.float32)
    own_back = back_chain(prep_out[0], prep_out[3], cotangent)
    flipped = jnp.swapaxes(carry_map, 1, 2)
    later_grad = shifted_2(affine_scan(flipped, own_back, "seq", -1), "seq", -1)
    chain_grads = chain_pull((cotangent, later_grad))
    delta_grads = (None,) + prep_pull(tuple(chain_grads[1:]))
    value_grad = jnp.swapaxes(delta_grads[3], 0, 1).astype(jnp.float32)
    weighted = value_grad * norm_gain[None]
    dot_part = jnp.sum(weighted * attended, axis=(1, 2))
    gain_part = jnp.sum(value_grad * scaled, axis=0)
    dot_all = lax.psum(dot_part, "head")
    gain_grad = butterfly_sum(gain_part, "seq")
    attended_grad = (
        inverse[:, None, None] * weighted
        - attended * (inverse * inverse * inverse * dot_all / features)[:, None, None]
    )
    query_grad, keys_grad, values_grad = attention_pull(attended_grad)
    own_key_grad = keys_grad[WIN:]
    own_value_grad = values_grad[WIN:]
    extra_key = jnp.zeros((rim_rows, head_count, head_width), jnp.float32)
    extra_value = jnp.zeros((rim_rows, head_count, head_width), jnp.float32)
    for offset in range(reach_back):
        segment = reach_back - 1 - offset
        sent_key = keys_grad[segment * rim_rows : (segment + 1) * rim_rows]
        sent_value = values_grad[segment * rim_rows : (segment + 1) * rim_rows]
        came = shifted_2(
            jnp.concatenate([sent_key, sent_value], axis=-1).astype(jnp.bfloat16),
            "seq",
            -(offset + 1),
        ).astype(sent_key.dtype)
        came_key = came[..., :head_width]
        came_value = came[..., head_width:]
        extra_key = extra_key + came_key
        extra_value = extra_value + came_value
    own_key_grad = own_key_grad.at[row_count - rim_rows :].add(extra_key)
    own_value_grad = own_value_grad.at[row_count - rim_rows :].add(extra_value)
    block_out = jnp.swapaxes(state_output, 0, 1).astype(jnp.bfloat16)
    return (
        block_out,
        query_grad.astype(jnp.bfloat16),
        own_key_grad.astype(jnp.bfloat16),
        own_value_grad.astype(jnp.bfloat16),
        gain_grad,
        jnp.swapaxes(delta_grads[1], 0, 1).astype(jnp.bfloat16),
        jnp.swapaxes(delta_grads[2], 0, 1).astype(jnp.bfloat16),
        delta_grads[4].T,
        delta_grads[5].T,
    )


def solution(mesh):
    return jax.shard_map(
        body,
        mesh=mesh,
        in_specs=(
            P("seq", "head", None),
            P("seq", "head", None),
            P("seq", "head", None),
            P("head", None),
            P("seq", "head", None),
            P("seq", "head", None),
            P("seq", "head"),
            P("seq", "head"),
            P("seq", "head", None),
        ),
        out_specs=(
            P("seq", "head", None),
            P("seq", "head", None),
            P("seq", "head", None),
            P("seq", "head", None),
            P("head", None),
            P("seq", "head", None),
            P("seq", "head", None),
            P("seq", "head"),
            P("seq", "head"),
        ),
        check_vma=False,
    )
```

```python
import jax
import jax.numpy as jnp
from jax import lax
from jax.sharding import PartitionSpec as P

WIN = 1024
CH = 64


MATMUL_ACCURACY = lax.Precision.HIGHEST
EPSILON = 1e-06


def shifted_2(block, axis, distance):
    devices = range(lax.axis_size(axis))
    route = [(i - distance, i) for i in devices if i - distance in devices]
    return lax.ppermute(block, axis, route)


def scan_maps(mat, axis, direction):
    size = lax.axis_size(axis)
    levels = []
    distance = 1
    while distance < size:
        levels.append(mat)
        if 2 * distance < size:
            mat = apply_map(mat, shifted_2(mat, axis, direction * distance))
        distance *= 2
    return levels


def scan_vectors(levels, vec, axis, direction):
    distance = 1
    for mat in levels:
        vec = apply_map(mat, shifted_2(vec, axis, direction * distance)) + vec
        distance *= 2
    return vec


def butterfly_sum(block, axis):
    size = lax.axis_size(axis)
    if size & (size - 1):
        return lax.psum(block, axis)
    distance = 1
    while distance < size:
        route = [(i, i ^ distance) for i in range(size)]
        block = block + lax.ppermute(block, axis, route)
        distance *= 2
    return block


def unit_rows(matrix):
    return matrix * lax.rsqrt(jnp.sum(matrix * matrix, axis=-1, keepdims=True) + EPSILON)


def delta_block(memory_state, pieces):
    query_vectors, key_vectors, value_rows, rate_rows, decay_rows = pieces
    length = key_vectors.shape[1]
    lower = jnp.tril(jnp.ones((length, length), jnp.float32))
    strict = lower - jnp.eye(length, dtype=jnp.float32)
    running_state = jnp.cumsum(decay_rows, axis=1)
    ratio = jnp.exp((running_state[:, :, None] - running_state[:, None, :]) * lower) * lower
    state_increment = jnp.exp(running_state)
    intersection = jnp.einsum("htk,hsk->hts", key_vectors, key_vectors, precision=MATMUL_ACCURACY)
    system = (
        jnp.eye(length, dtype=jnp.float32) + rate_rows[:, :, None] * ratio * strict * intersection
    )
    retrieved_values = jnp.einsum(
        "nex,nxp->nep", key_vectors, memory_state, precision=MATMUL_ACCURACY
    )
    target = rate_rows[:, :, None] * (value_rows - state_increment[:, :, None] * retrieved_values)
    newest_state = jax.scipy.linalg.solve_triangular(system, target, lower=True, unit_diagonal=True)
    local_scores = (
        jnp.einsum("htk,hsk->hts", query_vectors, key_vectors, precision=MATMUL_ACCURACY) * ratio
    )
    state_output = state_increment[:, :, None] * jnp.einsum(
        "nex,nxp->nep", query_vectors, memory_state, precision=MATMUL_ACCURACY
    )
    state_output = state_output + jnp.einsum(
        "hts,hsv->htv", local_scores, newest_state, precision=MATMUL_ACCURACY
    )
    retained_state = jnp.exp(running_state[:, -1:] - running_state)
    memory_state = jnp.exp(running_state[:, -1])[:, None, None] * memory_state + jnp.einsum(
        "wpa,wpn->wan",
        key_vectors * retained_state[:, :, None],
        newest_state,
        precision=MATMUL_ACCURACY,
    )
    return (memory_state, state_output)


def delta_sweep(memory_state, query_vectors, key_vectors, value_rows, rate_rows, decay_rows):
    head_count, length = (key_vectors.shape[0], key_vectors.shape[1])
    blocks = length // CH

    def cut_blocks(array):
        return jnp.moveaxis(array.reshape((head_count, blocks, CH) + array.shape[2:]), 1, 0)

    last_state, state_output = lax.scan(
        delta_block,
        memory_state,
        (
            cut_blocks(query_vectors),
            cut_blocks(key_vectors),
            cut_blocks(value_rows),
            cut_blocks(rate_rows),
            cut_blocks(decay_rows),
        ),
    )
    return (
        last_state,
        jnp.moveaxis(state_output, 0, 1).reshape(head_count, length, state_output.shape[-1]),
    )


def block_prep(query_heads, key_heads, value_heads, rate_heads, decay_heads):
    head_count, length, width = key_heads.shape
    blocks = length // CH

    def cut(array):
        return array.reshape((head_count, blocks, CH) + array.shape[2:])

    query_vectors = cut(unit_rows(query_heads))
    key_vectors = cut(unit_rows(key_heads))
    value_rows = cut(value_heads.astype(jnp.float32))
    rate_rows = cut(rate_heads)
    running_state = jnp.cumsum(cut(decay_heads), axis=-1)
    lower = jnp.tril(jnp.ones((CH, CH), jnp.float32))
    strict = lower - jnp.eye(CH, dtype=jnp.float32)
    ratio = jnp.exp((running_state[..., :, None] - running_state[..., None, :]) * lower) * lower
    state_increment = jnp.exp(running_state)
    intersection = jnp.einsum(
        "hbtk,hbsk->hbts", key_vectors, key_vectors, precision=MATMUL_ACCURACY
    )
    system = jnp.eye(CH, dtype=jnp.float32) + rate_rows[..., None] * ratio * strict * intersection
    inverse = jax.scipy.linalg.solve_triangular(
        system,
        jnp.broadcast_to(jnp.eye(CH, dtype=jnp.float32), system.shape),
        lower=True,
        unit_diagonal=True,
    )
    fresh = jnp.einsum(
        "hbts,hbsv->hbtv", inverse, rate_rows[..., None] * value_rows, precision=MATMUL_ACCURACY
    )
    pulled = jnp.einsum(
        "hbts,hbsk->hbtk",
        inverse,
        (rate_rows * state_increment)[..., None] * key_vectors,
        precision=MATMUL_ACCURACY,
    )
    local_scores = (
        jnp.einsum("hbtk,hbsk->hbts", query_vectors, key_vectors, precision=MATMUL_ACCURACY)
        * ratio
    )
    base_out = jnp.einsum("hbts,hbsv->hbtv", local_scores, fresh, precision=MATMUL_ACCURACY)
    read_map = state_increment[..., None] * query_vectors - jnp.einsum(
        "hbts,hbsk->hbtk", local_scores, pulled, precision=MATMUL_ACCURACY
    )
    retained = key_vectors * jnp.exp(running_state[..., -1:] - running_state)[..., None]
    step_map = jnp.exp(running_state[..., -1])[..., None, None] * jnp.eye(
        width, dtype=jnp.float32
    ) - jnp.einsum("hbtk,hbtj->hbkj", retained, pulled, precision=MATMUL_ACCURACY)
    step_add = jnp.einsum("hbtk,hbtv->hbkv", retained, fresh, precision=MATMUL_ACCURACY)
    return (step_map, step_add, base_out, read_map)


def summarize(step_map, step_add):
    carry_map = step_map[:, 0]
    carry_add = step_add[:, 0]
    for block in range(1, step_map.shape[1]):
        carry_add = apply_map(step_map[:, block], carry_add) + step_add[:, block]
        carry_map = apply_map(step_map[:, block], carry_map)
    return (carry_map, carry_add)


def local_chain(start_state, step_map, step_add, base_out, read_map):
    state = start_state
    outputs = []
    for block in range(step_map.shape[1]):
        outputs.append(base_out[:, block] + apply_map(read_map[:, block], state))
        state = apply_map(step_map[:, block], state) + step_add[:, block]
    return (jnp.concatenate(outputs, axis=1), state)


def back_chain(step_map, read_map, cotangent):
    blocks = step_map.shape[1]
    pieces = cotangent.reshape((cotangent.shape[0], blocks, CH) + cotangent.shape[2:])
    start_grad = None
    for block in reversed(range(blocks)):
        term = jnp.einsum(
            "htk,htv->hkv", read_map[:, block], pieces[:, block], precision=MATMUL_ACCURACY
        )
        if start_grad is not None:
            term = term + apply_map(jnp.swapaxes(step_map[:, block], 1, 2), start_grad)
        start_grad = term
    return start_grad


def window_softmax(rows_here, keys_here, values_here, alive_keys):
    block_rows = rows_here.shape[0]
    span_rows = keys_here.shape[0]
    reach_back = span_rows - block_rows
    scores = jnp.einsum("qhd,khd->hqk", rows_here, keys_here) * rows_here.shape[-1] ** (-0.5)
    query_pos = jnp.arange(block_rows, dtype=jnp.int32)[:, None]
    key_pos = jnp.arange(span_rows, dtype=jnp.int32)[None, :]
    allowed = (key_pos > query_pos) & (key_pos <= query_pos + reach_back) & alive_keys[None, :]
    scores = jnp.where(allowed[None], scores, -1e30)
    shifted = jnp.exp(scores - jnp.max(scores, axis=-1, keepdims=True))
    weights_bf = (shifted / jnp.sum(shifted, axis=-1, keepdims=True)).astype(jnp.bfloat16)
    return jnp.einsum("hqk,khd->qhd", weights_bf.astype(jnp.float32), values_here)


def attend(query_vectors, key_vectors, value_rows, alive_keys):
    outputs = [window_softmax(query_vectors, key_vectors, value_rows, alive_keys)]
    return jnp.concatenate(outputs, axis=0)


def apply_map(matrix, operand):
    return jnp.einsum("hij,hjv->hiv", matrix, operand, precision=MATMUL_ACCURACY)


def body(
    att_query, att_key, att_value, norm_gain, dn_query, dn_key, write_rate, log_decay, out_grad
):
    row_count, head_count, head_width = att_query.shape
    rim_rows = min(WIN, row_count)
    reach_back = max(1, WIN // row_count)
    my_shard = lax.axis_index("seq")
    shard_count = lax.axis_size("seq")
    older_keys = []
    older_values = []
    key_value = jnp.concatenate([att_key, att_value], axis=-1)
    for offset in range(reach_back):
        came = shifted_2(key_value, "seq", offset + 1)
        older_keys.insert(0, came[..., :head_width])
        older_values.insert(0, came[..., head_width:])
    all_keys = jnp.concatenate(older_keys + [att_key], axis=0).astype(jnp.float32)
    all_values = jnp.concatenate(older_values + [att_value], axis=0).astype(jnp.float32)
    alive_keys = my_shard * row_count - WIN + jnp.arange(WIN + row_count, dtype=jnp.int32) >= 0

    def attention_core(query_vectors, key_vectors, value_rows):
        return attend(query_vectors, key_vectors, value_rows, alive_keys)

    attended, attention_pull = jax.vjp(
        attention_core, att_query.astype(jnp.float32), all_keys, all_values
    )
    square_part = jnp.sum(attended * attended, axis=(1, 2))
    square_all = lax.psum(square_part, "head")
    features = head_count * lax.axis_size("head") * head_width
    inverse = lax.rsqrt(square_all / features + EPSILON)
    scaled = attended * inverse[:, None, None]
    values = (scaled * norm_gain[None]).astype(jnp.bfloat16)
    query_heads = jnp.swapaxes(dn_query, 0, 1).astype(jnp.float32)
    key_heads = jnp.swapaxes(dn_key, 0, 1).astype(jnp.float32)
    value_heads = jnp.swapaxes(values, 0, 1)
    rate_heads = write_rate.T
    decay_heads = log_decay.T
    prep_out, prep_pull = jax.vjp(
        block_prep, query_heads, key_heads, value_heads, rate_heads, decay_heads
    )
    carry_map, carry_add = summarize(prep_out[0], prep_out[1])
    empty_state = jnp.zeros_like(carry_add)
    start_state = shifted_2(
        scan_vectors(scan_maps(carry_map, "seq", 1), carry_add, "seq", 1), "seq", 1
    )
    (state_output, last_state), chain_pull = jax.vjp(local_chain, start_state, *prep_out)
    cotangent = jnp.swapaxes(out_grad, 0, 1).astype(jnp.float32)
    own_back = back_chain(prep_out[0], prep_out[3], cotangent)
    flipped = jnp.swapaxes(carry_map, 1, 2)
    later_grad = shifted_2(
        scan_vectors(scan_maps(flipped, "seq", -1), own_back, "seq", -1), "seq", -1
    )
    chain_grads = chain_pull((cotangent, later_grad))
    delta_grads = (None,) + prep_pull(tuple(chain_grads[1:]))
    value_grad = jnp.swapaxes(delta_grads[3], 0, 1).astype(jnp.float32)
    weighted = value_grad * norm_gain[None]
    dot_part = jnp.sum(weighted * attended, axis=(1, 2))
    gain_part = jnp.sum(value_grad * scaled, axis=0)
    dot_all = lax.psum(dot_part, "head")
    gain_grad = butterfly_sum(gain_part, "seq")
    attended_grad = (
        inverse[:, None, None] * weighted
        - attended * (inverse * inverse * inverse * dot_all / features)[:, None, None]
    )
    query_grad, keys_grad, values_grad = attention_pull(attended_grad)
    own_key_grad = keys_grad[WIN:]
    own_value_grad = values_grad[WIN:]
    extra_key = jnp.zeros((rim_rows, head_count, head_width), jnp.float32)
    extra_value = jnp.zeros((rim_rows, head_count, head_width), jnp.float32)
    for offset in range(reach_back):
        segment = reach_back - 1 - offset
        sent_key = keys_grad[segment * rim_rows : (segment + 1) * rim_rows]
        sent_value = values_grad[segment * rim_rows : (segment + 1) * rim_rows]
        came = shifted_2(
            jnp.concatenate([sent_key, sent_value], axis=-1).astype(jnp.bfloat16),
            "seq",
            -(offset + 1),
        ).astype(sent_key.dtype)
        came_key = came[..., :head_width]
        came_value = came[..., head_width:]
        extra_key = extra_key + came_key
        extra_value = extra_value + came_value
    own_key_grad = own_key_grad.at[row_count - rim_rows :].add(extra_key)
    own_value_grad = own_value_grad.at[row_count - rim_rows :].add(extra_value)
    block_out = jnp.swapaxes(state_output, 0, 1).astype(jnp.bfloat16)
    return (
        block_out,
        query_grad.astype(jnp.bfloat16),
        own_key_grad.astype(jnp.bfloat16),
        own_value_grad.astype(jnp.bfloat16),
        gain_grad,
        jnp.swapaxes(delta_grads[1], 0, 1).astype(jnp.bfloat16),
        jnp.swapaxes(delta_grads[2], 0, 1).astype(jnp.bfloat16),
        delta_grads[4].T,
        delta_grads[5].T,
    )


def solution(mesh):
    return jax.shard_map(
        body,
        mesh=mesh,
        in_specs=(
            P("seq", "head", None),
            P("seq", "head", None),
            P("seq", "head", None),
            P("head", None),
            P("seq", "head", None),
            P("seq", "head", None),
            P("seq", "head"),
            P("seq", "head"),
            P("seq", "head", None),
        ),
        out_specs=(
            P("seq", "head", None),
            P("seq", "head", None),
            P("seq", "head", None),
            P("seq", "head", None),
            P("head", None),
            P("seq", "head", None),
            P("seq", "head", None),
            P("seq", "head"),
            P("seq", "head"),
        ),
        check_vma=False,
    )
```

```python
import jax
import jax.numpy as jnp
from jax import lax
from jax.sharding import PartitionSpec as P

WIN = 1024
CH = 64


MATMUL_ACCURACY = lax.Precision.HIGHEST
EPSILON = 1e-06


def shifted_2(block, axis, distance):
    devices = range(lax.axis_size(axis))
    route = [(i - distance, i) for i in devices if i - distance in devices]
    return lax.ppermute(block, axis, route)


def affine_scan(mat, vec, axis, direction):
    size = lax.axis_size(axis)
    distance = 1
    while distance < size:
        if 2 * distance >= size:
            came_vec = shifted_2(vec, axis, direction * distance)
            vec = apply_map(mat, came_vec) + vec
        else:
            came = shifted_2(jnp.concatenate([mat, vec], axis=-1), axis, direction * distance)
            came_mat = came[..., : mat.shape[-1]]
            came_vec = came[..., mat.shape[-1] :]
            vec = apply_map(mat, came_vec) + vec
            mat = apply_map(mat, came_mat)
        distance *= 2
    return vec


def butterfly_sum(block, axis):
    size = lax.axis_size(axis)
    if size & (size - 1):
        return lax.psum(block, axis)
    distance = 1
    while distance < size:
        route = [(i, i ^ distance) for i in range(size)]
        block = block + lax.ppermute(block, axis, route)
        distance *= 2
    return block


def unit_rows(matrix):
    return matrix * lax.rsqrt(jnp.sum(matrix * matrix, axis=-1, keepdims=True) + EPSILON)


def delta_block(memory_state, pieces):
    query_vectors, key_vectors, value_rows, rate_rows, decay_rows = pieces
    length = key_vectors.shape[1]
    lower = jnp.tril(jnp.ones((length, length), jnp.float32))
    strict = lower - jnp.eye(length, dtype=jnp.float32)
    running_state = jnp.cumsum(decay_rows, axis=1)
    ratio = jnp.exp((running_state[:, :, None] - running_state[:, None, :]) * lower) * lower
    state_increment = jnp.exp(running_state)
    intersection = jnp.einsum("htk,hsk->hts", key_vectors, key_vectors, precision=MATMUL_ACCURACY)
    system = (
        jnp.eye(length, dtype=jnp.float32) + rate_rows[:, :, None] * ratio * strict * intersection
    )
    retrieved_values = jnp.einsum(
        "nex,nxp->nep", key_vectors, memory_state, precision=MATMUL_ACCURACY
    )
    target = rate_rows[:, :, None] * (value_rows - state_increment[:, :, None] * retrieved_values)
    newest_state = jax.scipy.linalg.solve_triangular(system, target, lower=True, unit_diagonal=True)
    local_scores = (
        jnp.einsum("htk,hsk->hts", query_vectors, key_vectors, precision=MATMUL_ACCURACY) * ratio
    )
    state_output = state_increment[:, :, None] * jnp.einsum(
        "nex,nxp->nep", query_vectors, memory_state, precision=MATMUL_ACCURACY
    )
    state_output = state_output + jnp.einsum(
        "hts,hsv->htv", local_scores, newest_state, precision=MATMUL_ACCURACY
    )
    retained_state = jnp.exp(running_state[:, -1:] - running_state)
    memory_state = jnp.exp(running_state[:, -1])[:, None, None] * memory_state + jnp.einsum(
        "wpa,wpn->wan",
        key_vectors * retained_state[:, :, None],
        newest_state,
        precision=MATMUL_ACCURACY,
    )
    return (memory_state, state_output)


def delta_sweep(memory_state, query_vectors, key_vectors, value_rows, rate_rows, decay_rows):
    head_count, length = (key_vectors.shape[0], key_vectors.shape[1])
    blocks = length // CH

    def cut_blocks(array):
        return jnp.moveaxis(array.reshape((head_count, blocks, CH) + array.shape[2:]), 1, 0)

    last_state, state_output = lax.scan(
        delta_block,
        memory_state,
        (
            cut_blocks(query_vectors),
            cut_blocks(key_vectors),
            cut_blocks(value_rows),
            cut_blocks(rate_rows),
            cut_blocks(decay_rows),
        ),
    )
    return (
        last_state,
        jnp.moveaxis(state_output, 0, 1).reshape(head_count, length, state_output.shape[-1]),
    )


def block_prep(query_heads, key_heads, value_heads, rate_heads, decay_heads):
    head_count, length, width = key_heads.shape
    blocks = length // CH

    def cut(array):
        return array.reshape((head_count, blocks, CH) + array.shape[2:])

    query_vectors = cut(unit_rows(query_heads))
    key_vectors = cut(unit_rows(key_heads))
    value_rows = cut(value_heads.astype(jnp.float32))
    rate_rows = cut(rate_heads)
    running_state = jnp.cumsum(cut(decay_heads), axis=-1)
    lower = jnp.tril(jnp.ones((CH, CH), jnp.float32))
    strict = lower - jnp.eye(CH, dtype=jnp.float32)
    ratio = jnp.exp((running_state[..., :, None] - running_state[..., None, :]) * lower) * lower
    state_increment = jnp.exp(running_state)
    intersection = jnp.einsum(
        "hbtk,hbsk->hbts", key_vectors, key_vectors, precision=MATMUL_ACCURACY
    )
    system = jnp.eye(CH, dtype=jnp.float32) + rate_rows[..., None] * ratio * strict * intersection
    sides = jnp.concatenate(
        [
            rate_rows[..., None] * value_rows,
            (rate_rows * state_increment)[..., None] * key_vectors,
        ],
        axis=-1,
    )
    solved = jax.scipy.linalg.solve_triangular(system, sides, lower=True, unit_diagonal=True)
    fresh = solved[..., : value_rows.shape[-1]]
    pulled = solved[..., value_rows.shape[-1] :]
    local_scores = (
        jnp.einsum("hbtk,hbsk->hbts", query_vectors, key_vectors, precision=MATMUL_ACCURACY)
        * ratio
    )
    base_out = jnp.einsum("hbts,hbsv->hbtv", local_scores, fresh, precision=MATMUL_ACCURACY)
    read_map = state_increment[..., None] * query_vectors - jnp.einsum(
        "hbts,hbsk->hbtk", local_scores, pulled, precision=MATMUL_ACCURACY
    )
    retained = key_vectors * jnp.exp(running_state[..., -1:] - running_state)[..., None]
    step_map = jnp.exp(running_state[..., -1])[..., None, None] * jnp.eye(
        width, dtype=jnp.float32
    ) - jnp.einsum("hbtk,hbtj->hbkj", retained, pulled, precision=MATMUL_ACCURACY)
    step_add = jnp.einsum("hbtk,hbtv->hbkv", retained, fresh, precision=MATMUL_ACCURACY)
    return (step_map, step_add, base_out, read_map)


def summarize(step_map, step_add):
    carry_map = step_map[:, 0]
    carry_add = step_add[:, 0]
    for block in range(1, step_map.shape[1]):
        carry_add = apply_map(step_map[:, block], carry_add) + step_add[:, block]
        carry_map = apply_map(step_map[:, block], carry_map)
    return (carry_map, carry_add)


def local_chain(start_state, step_map, step_add, base_out, read_map):
    state = start_state
    outputs = []
    for block in range(step_map.shape[1]):
        outputs.append(base_out[:, block] + apply_map(read_map[:, block], state))
        state = apply_map(step_map[:, block], state) + step_add[:, block]
    return (jnp.concatenate(outputs, axis=1), state)


def back_chain(step_map, read_map, cotangent):
    blocks = step_map.shape[1]
    pieces = cotangent.reshape((cotangent.shape[0], blocks, CH) + cotangent.shape[2:])
    start_grad = None
    for block in reversed(range(blocks)):
        term = jnp.einsum(
            "htk,htv->hkv", read_map[:, block], pieces[:, block], precision=MATMUL_ACCURACY
        )
        if start_grad is not None:
            term = term + apply_map(jnp.swapaxes(step_map[:, block], 1, 2), start_grad)
        start_grad = term
    return start_grad


def window_softmax(rows_here, keys_here, values_here, alive_keys):
    block_rows = rows_here.shape[0]
    span_rows = keys_here.shape[0]
    reach_back = span_rows - block_rows
    scores = jnp.einsum("qhd,khd->hqk", rows_here, keys_here) * rows_here.shape[-1] ** (-0.5)
    query_pos = jnp.arange(block_rows, dtype=jnp.int32)[:, None]
    key_pos = jnp.arange(span_rows, dtype=jnp.int32)[None, :]
    allowed = (key_pos > query_pos) & (key_pos <= query_pos + reach_back) & alive_keys[None, :]
    scores = jnp.where(allowed[None], scores, -1e30)
    shifted = jnp.exp(scores - jnp.max(scores, axis=-1, keepdims=True))
    weights_bf = (shifted / jnp.sum(shifted, axis=-1, keepdims=True)).astype(jnp.bfloat16)
    return jnp.einsum("hqk,khd->qhd", weights_bf.astype(jnp.float32), values_here)


def attend(query_vectors, key_vectors, value_rows, alive_keys):
    outputs = [window_softmax(query_vectors, key_vectors, value_rows, alive_keys)]
    return jnp.concatenate(outputs, axis=0)


def apply_map(matrix, operand):
    return jnp.einsum("hij,hjv->hiv", matrix, operand, precision=MATMUL_ACCURACY)


def body(
    att_query, att_key, att_value, norm_gain, dn_query, dn_key, write_rate, log_decay, out_grad
):
    row_count, head_count, head_width = att_query.shape
    rim_rows = min(WIN, row_count)
    reach_back = max(1, WIN // row_count)
    my_shard = lax.axis_index("seq")
    shard_count = lax.axis_size("seq")
    older_keys = []
    older_values = []
    key_value = jnp.concatenate([att_key, att_value], axis=-1)
    for offset in range(reach_back):
        came = shifted_2(key_value, "seq", offset + 1)
        older_keys.insert(0, came[..., :head_width])
        older_values.insert(0, came[..., head_width:])
    all_keys = jnp.concatenate(older_keys + [att_key], axis=0).astype(jnp.float32)
    all_values = jnp.concatenate(older_values + [att_value], axis=0).astype(jnp.float32)
    alive_keys = my_shard * row_count - WIN + jnp.arange(WIN + row_count, dtype=jnp.int32) >= 0

    def attention_core(query_vectors, key_vectors, value_rows):
        return attend(query_vectors, key_vectors, value_rows, alive_keys)

    attended, attention_pull = jax.vjp(
        attention_core, att_query.astype(jnp.float32), all_keys, all_values
    )
    square_part = jnp.sum(attended * attended, axis=(1, 2))
    square_all = lax.psum(square_part, "head")
    features = head_count * lax.axis_size("head") * head_width
    inverse = lax.rsqrt(square_all / features + EPSILON)
    scaled = attended * inverse[:, None, None]
    values = (scaled * norm_gain[None]).astype(jnp.bfloat16)
    query_heads = jnp.swapaxes(dn_query, 0, 1).astype(jnp.float32)
    key_heads = jnp.swapaxes(dn_key, 0, 1).astype(jnp.float32)
    value_heads = jnp.swapaxes(values, 0, 1)
    rate_heads = write_rate.T
    decay_heads = log_decay.T
    prep_out, prep_pull = jax.vjp(
        block_prep, query_heads, key_heads, value_heads, rate_heads, decay_heads
    )
    carry_map, carry_add = summarize(prep_out[0], prep_out[1])
    empty_state = jnp.zeros_like(carry_add)
    start_state = shifted_2(affine_scan(carry_map, carry_add, "seq", 1), "seq", 1)
    (state_output, last_state), chain_pull = jax.vjp(local_chain, start_state, *prep_out)
    cotangent = jnp.swapaxes(out_grad, 0, 1).astype(jnp.float32)
    own_back = back_chain(prep_out[0], prep_out[3], cotangent)
    flipped = jnp.swapaxes(carry_map, 1, 2)
    later_grad = shifted_2(affine_scan(flipped, own_back, "seq", -1), "seq", -1)
    chain_grads = chain_pull((cotangent, later_grad))
    delta_grads = (None,) + prep_pull(tuple(chain_grads[1:]))
    value_grad = jnp.swapaxes(delta_grads[3], 0, 1).astype(jnp.float32)
    weighted = value_grad * norm_gain[None]
    dot_part = jnp.sum(weighted * attended, axis=(1, 2))
    gain_part = jnp.sum(value_grad * scaled, axis=0)
    dot_all = lax.psum(dot_part, "head")
    gain_grad = butterfly_sum(gain_part, "seq")
    attended_grad = (
        inverse[:, None, None] * weighted
        - attended * (inverse * inverse * inverse * dot_all / features)[:, None, None]
    )
    query_grad, keys_grad, values_grad = attention_pull(attended_grad)
    own_key_grad = keys_grad[WIN:]
    own_value_grad = values_grad[WIN:]
    extra_key = jnp.zeros((rim_rows, head_count, head_width), jnp.float32)
    extra_value = jnp.zeros((rim_rows, head_count, head_width), jnp.float32)
    for offset in range(reach_back):
        segment = reach_back - 1 - offset
        sent_key = keys_grad[segment * rim_rows : (segment + 1) * rim_rows]
        sent_value = values_grad[segment * rim_rows : (segment + 1) * rim_rows]
        came = shifted_2(
            jnp.concatenate([sent_key, sent_value], axis=-1).astype(jnp.bfloat16),
            "seq",
            -(offset + 1),
        ).astype(sent_key.dtype)
        came_key = came[..., :head_width]
        came_value = came[..., head_width:]
        extra_key = extra_key + came_key
        extra_value = extra_value + came_value
    own_key_grad = own_key_grad.at[row_count - rim_rows :].add(extra_key)
    own_value_grad = own_value_grad.at[row_count - rim_rows :].add(extra_value)
    block_out = jnp.swapaxes(state_output, 0, 1).astype(jnp.bfloat16)
    return (
        block_out,
        query_grad.astype(jnp.bfloat16),
        own_key_grad.astype(jnp.bfloat16),
        own_value_grad.astype(jnp.bfloat16),
        gain_grad,
        jnp.swapaxes(delta_grads[1], 0, 1).astype(jnp.bfloat16),
        jnp.swapaxes(delta_grads[2], 0, 1).astype(jnp.bfloat16),
        delta_grads[4].T,
        delta_grads[5].T,
    )


def solution(mesh):
    return jax.shard_map(
        body,
        mesh=mesh,
        in_specs=(
            P("seq", "head", None),
            P("seq", "head", None),
            P("seq", "head", None),
            P("head", None),
            P("seq", "head", None),
            P("seq", "head", None),
            P("seq", "head"),
            P("seq", "head"),
            P("seq", "head", None),
        ),
        out_specs=(
            P("seq", "head", None),
            P("seq", "head", None),
            P("seq", "head", None),
            P("seq", "head", None),
            P("head", None),
            P("seq", "head", None),
            P("seq", "head", None),
            P("seq", "head"),
            P("seq", "head"),
        ),
        check_vma=False,
    )
```

```python
import jax
import jax.numpy as jnp
from jax import lax
from jax.sharding import PartitionSpec as P

WIN = 1024
CH = 64


MATMUL_ACCURACY = lax.Precision.HIGHEST
EPSILON = 1e-06


def shifted_2(block, axis, distance):
    devices = range(lax.axis_size(axis))
    route = [(i - distance, i) for i in devices if i - distance in devices]
    return lax.ppermute(block, axis, route)


def affine_scan(mat, vec, axis, direction):
    size = lax.axis_size(axis)
    distance = 1
    while distance < size:
        if 2 * distance >= size:
            came_vec = shifted_2(vec, axis, direction * distance)
            vec = apply_map(mat, came_vec) + vec
        else:
            came_mat, came_vec = shifted_2((mat, vec), axis, direction * distance)
            vec = apply_map(mat, came_vec) + vec
            mat = apply_map(mat, came_mat)
        distance *= 2
    return vec


def paired_scans(forward_mat, forward_vec, backward_mat, backward_vec, axis):
    size = lax.axis_size(axis)
    distance = 1
    while distance < size:
        stepped = []
        for direction, mat, vec in (
            (1, forward_mat, forward_vec),
            (-1, backward_mat, backward_vec),
        ):
            if 2 * distance >= size:
                came_vec = shifted_2(vec, axis, direction * distance)
                vec = apply_map(mat, came_vec) + vec
            else:
                came_mat, came_vec = shifted_2((mat, vec), axis, direction * distance)
                vec = apply_map(mat, came_vec) + vec
                mat = apply_map(mat, came_mat)
            stepped.append((mat, vec))
        (forward_mat, forward_vec), (backward_mat, backward_vec) = lax.optimization_barrier(
            tuple(stepped)
        )
        distance *= 2
    return (shifted_2(forward_vec, axis, 1), shifted_2(backward_vec, axis, -1))


def butterfly_sum(block, axis):
    size = lax.axis_size(axis)
    if size & (size - 1):
        return lax.psum(block, axis)
    distance = 1
    while distance < size:
        route = [(i, i ^ distance) for i in range(size)]
        block = block + lax.ppermute(block, axis, route)
        distance *= 2
    return block


def unit_rows(matrix):
    return matrix * lax.rsqrt(jnp.sum(matrix * matrix, axis=-1, keepdims=True) + EPSILON)


def delta_block(memory_state, pieces):
    query_vectors, key_vectors, value_rows, rate_rows, decay_rows = pieces
    length = key_vectors.shape[1]
    lower = jnp.tril(jnp.ones((length, length), jnp.float32))
    strict = lower - jnp.eye(length, dtype=jnp.float32)
    running_state = jnp.cumsum(decay_rows, axis=1)
    ratio = jnp.exp((running_state[:, :, None] - running_state[:, None, :]) * lower) * lower
    state_increment = jnp.exp(running_state)
    intersection = jnp.einsum("htk,hsk->hts", key_vectors, key_vectors, precision=MATMUL_ACCURACY)
    system = (
        jnp.eye(length, dtype=jnp.float32) + rate_rows[:, :, None] * ratio * strict * intersection
    )
    retrieved_values = jnp.einsum(
        "nex,nxp->nep", key_vectors, memory_state, precision=MATMUL_ACCURACY
    )
    target = rate_rows[:, :, None] * (value_rows - state_increment[:, :, None] * retrieved_values)
    newest_state = jax.scipy.linalg.solve_triangular(system, target, lower=True, unit_diagonal=True)
    local_scores = (
        jnp.einsum("htk,hsk->hts", query_vectors, key_vectors, precision=MATMUL_ACCURACY) * ratio
    )
    state_output = state_increment[:, :, None] * jnp.einsum(
        "nex,nxp->nep", query_vectors, memory_state, precision=MATMUL_ACCURACY
    )
    state_output = state_output + jnp.einsum(
        "hts,hsv->htv", local_scores, newest_state, precision=MATMUL_ACCURACY
    )
    retained_state = jnp.exp(running_state[:, -1:] - running_state)
    memory_state = jnp.exp(running_state[:, -1])[:, None, None] * memory_state + jnp.einsum(
        "wpa,wpn->wan",
        key_vectors * retained_state[:, :, None],
        newest_state,
        precision=MATMUL_ACCURACY,
    )
    return (memory_state, state_output)


def delta_sweep(memory_state, query_vectors, key_vectors, value_rows, rate_rows, decay_rows):
    head_count, length = (key_vectors.shape[0], key_vectors.shape[1])
    blocks = length // CH

    def cut_blocks(array):
        return jnp.moveaxis(array.reshape((head_count, blocks, CH) + array.shape[2:]), 1, 0)

    last_state, state_output = lax.scan(
        delta_block,
        memory_state,
        (
            cut_blocks(query_vectors),
            cut_blocks(key_vectors),
            cut_blocks(value_rows),
            cut_blocks(rate_rows),
            cut_blocks(decay_rows),
        ),
    )
    return (
        last_state,
        jnp.moveaxis(state_output, 0, 1).reshape(head_count, length, state_output.shape[-1]),
    )


def block_prep(query_heads, key_heads, value_heads, rate_heads, decay_heads):
    head_count, length, width = key_heads.shape
    blocks = length // CH

    def cut(array):
        return array.reshape((head_count, blocks, CH) + array.shape[2:])

    query_vectors = cut(unit_rows(query_heads))
    key_vectors = cut(unit_rows(key_heads))
    value_rows = cut(value_heads.astype(jnp.float32))
    rate_rows = cut(rate_heads)
    running_state = jnp.cumsum(cut(decay_heads), axis=-1)
    lower = jnp.tril(jnp.ones((CH, CH), jnp.float32))
    strict = lower - jnp.eye(CH, dtype=jnp.float32)
    ratio = jnp.exp((running_state[..., :, None] - running_state[..., None, :]) * lower) * lower
    state_increment = jnp.exp(running_state)
    intersection = jnp.einsum(
        "hbtk,hbsk->hbts", key_vectors, key_vectors, precision=MATMUL_ACCURACY
    )
    system = jnp.eye(CH, dtype=jnp.float32) + rate_rows[..., None] * ratio * strict * intersection
    sides = jnp.concatenate(
        [
            rate_rows[..., None] * value_rows,
            (rate_rows * state_increment)[..., None] * key_vectors,
        ],
        axis=-1,
    )
    solved = jax.scipy.linalg.solve_triangular(system, sides, lower=True, unit_diagonal=True)
    fresh = solved[..., : value_rows.shape[-1]]
    pulled = solved[..., value_rows.shape[-1] :]
    local_scores = (
        jnp.einsum("hbtk,hbsk->hbts", query_vectors, key_vectors, precision=MATMUL_ACCURACY)
        * ratio
    )
    base_out = jnp.einsum("hbts,hbsv->hbtv", local_scores, fresh, precision=MATMUL_ACCURACY)
    read_map = state_increment[..., None] * query_vectors - jnp.einsum(
        "hbts,hbsk->hbtk", local_scores, pulled, precision=MATMUL_ACCURACY
    )
    retained = key_vectors * jnp.exp(running_state[..., -1:] - running_state)[..., None]
    step_map = jnp.exp(running_state[..., -1])[..., None, None] * jnp.eye(
        width, dtype=jnp.float32
    ) - jnp.einsum("hbtk,hbtj->hbkj", retained, pulled, precision=MATMUL_ACCURACY)
    step_add = jnp.einsum("hbtk,hbtv->hbkv", retained, fresh, precision=MATMUL_ACCURACY)
    return (step_map, step_add, base_out, read_map)


def summarize(step_map, step_add):
    carry_map = step_map[:, 0]
    carry_add = step_add[:, 0]
    for block in range(1, step_map.shape[1]):
        carry_add = apply_map(step_map[:, block], carry_add) + step_add[:, block]
        carry_map = apply_map(step_map[:, block], carry_map)
    return (carry_map, carry_add)


def local_chain(start_state, step_map, step_add, base_out, read_map):
    state = start_state
    outputs = []
    for block in range(step_map.shape[1]):
        outputs.append(base_out[:, block] + apply_map(read_map[:, block], state))
        state = apply_map(step_map[:, block], state) + step_add[:, block]
    return (jnp.concatenate(outputs, axis=1), state)


def back_chain(step_map, read_map, cotangent):
    blocks = step_map.shape[1]
    pieces = cotangent.reshape((cotangent.shape[0], blocks, CH) + cotangent.shape[2:])
    start_grad = None
    for block in reversed(range(blocks)):
        term = jnp.einsum(
            "htk,htv->hkv", read_map[:, block], pieces[:, block], precision=MATMUL_ACCURACY
        )
        if start_grad is not None:
            term = term + apply_map(jnp.swapaxes(step_map[:, block], 1, 2), start_grad)
        start_grad = term
    return start_grad


def window_softmax(rows_here, keys_here, values_here, alive_keys):
    block_rows = rows_here.shape[0]
    span_rows = keys_here.shape[0]
    reach_back = span_rows - block_rows
    scores = jnp.einsum("qhd,khd->hqk", rows_here, keys_here) * rows_here.shape[-1] ** (-0.5)
    query_pos = jnp.arange(block_rows, dtype=jnp.int32)[:, None]
    key_pos = jnp.arange(span_rows, dtype=jnp.int32)[None, :]
    allowed = (key_pos > query_pos) & (key_pos <= query_pos + reach_back) & alive_keys[None, :]
    scores = jnp.where(allowed[None], scores, -1e30)
    shifted = jnp.exp(scores - jnp.max(scores, axis=-1, keepdims=True))
    weights_bf = (shifted / jnp.sum(shifted, axis=-1, keepdims=True)).astype(jnp.bfloat16)
    return jnp.einsum("hqk,khd->qhd", weights_bf.astype(jnp.float32), values_here)


def attend(query_vectors, key_vectors, value_rows, alive_keys):
    outputs = [window_softmax(query_vectors, key_vectors, value_rows, alive_keys)]
    return jnp.concatenate(outputs, axis=0)


def apply_map(matrix, operand):
    return jnp.einsum("hij,hjv->hiv", matrix, operand, precision=MATMUL_ACCURACY)


def body(
    att_query, att_key, att_value, norm_gain, dn_query, dn_key, write_rate, log_decay, out_grad
):
    row_count, head_count, head_width = att_query.shape
    rim_rows = min(WIN, row_count)
    reach_back = max(1, WIN // row_count)
    my_shard = lax.axis_index("seq")
    shard_count = lax.axis_size("seq")
    older_keys = []
    older_values = []
    key_value = jnp.concatenate([att_key, att_value], axis=-1)
    for offset in range(reach_back):
        came = shifted_2(key_value, "seq", offset + 1)
        older_keys.insert(0, came[..., :head_width])
        older_values.insert(0, came[..., head_width:])
    all_keys = jnp.concatenate(older_keys + [att_key], axis=0).astype(jnp.float32)
    all_values = jnp.concatenate(older_values + [att_value], axis=0).astype(jnp.float32)
    alive_keys = my_shard * row_count - WIN + jnp.arange(WIN + row_count, dtype=jnp.int32) >= 0

    def attention_core(query_vectors, key_vectors, value_rows):
        return attend(query_vectors, key_vectors, value_rows, alive_keys)

    attended, attention_pull = jax.vjp(
        attention_core, att_query.astype(jnp.float32), all_keys, all_values
    )
    square_part = jnp.sum(attended * attended, axis=(1, 2))
    square_all = lax.psum(square_part, "head")
    features = head_count * lax.axis_size("head") * head_width
    inverse = lax.rsqrt(square_all / features + EPSILON)
    scaled = attended * inverse[:, None, None]
    values = (scaled * norm_gain[None]).astype(jnp.bfloat16)
    query_heads = jnp.swapaxes(dn_query, 0, 1).astype(jnp.float32)
    key_heads = jnp.swapaxes(dn_key, 0, 1).astype(jnp.float32)
    value_heads = jnp.swapaxes(values, 0, 1)
    rate_heads = write_rate.T
    decay_heads = log_decay.T
    prep_out, prep_pull = jax.vjp(
        block_prep, query_heads, key_heads, value_heads, rate_heads, decay_heads
    )
    carry_map, carry_add = summarize(prep_out[0], prep_out[1])
    empty_state = jnp.zeros_like(carry_add)
    cotangent = jnp.swapaxes(out_grad, 0, 1).astype(jnp.float32)
    own_back = back_chain(prep_out[0], prep_out[3], cotangent)
    flipped = jnp.swapaxes(carry_map, 1, 2)
    start_state, later_grad = paired_scans(carry_map, carry_add, flipped, own_back, "seq")
    (state_output, last_state), chain_pull = jax.vjp(local_chain, start_state, *prep_out)
    chain_grads = chain_pull((cotangent, later_grad))
    delta_grads = (None,) + prep_pull(tuple(chain_grads[1:]))
    value_grad = jnp.swapaxes(delta_grads[3], 0, 1).astype(jnp.float32)
    weighted = value_grad * norm_gain[None]
    dot_part = jnp.sum(weighted * attended, axis=(1, 2))
    gain_part = jnp.sum(value_grad * scaled, axis=0)
    dot_all = lax.psum(dot_part, "head")
    gain_grad = butterfly_sum(gain_part, "seq")
    attended_grad = (
        inverse[:, None, None] * weighted
        - attended * (inverse * inverse * inverse * dot_all / features)[:, None, None]
    )
    query_grad, keys_grad, values_grad = attention_pull(attended_grad)
    own_key_grad = keys_grad[WIN:]
    own_value_grad = values_grad[WIN:]
    extra_key = jnp.zeros((rim_rows, head_count, head_width), jnp.float32)
    extra_value = jnp.zeros((rim_rows, head_count, head_width), jnp.float32)
    for offset in range(reach_back):
        segment = reach_back - 1 - offset
        sent_key = keys_grad[segment * rim_rows : (segment + 1) * rim_rows]
        sent_value = values_grad[segment * rim_rows : (segment + 1) * rim_rows]
        came = shifted_2(
            jnp.concatenate([sent_key, sent_value], axis=-1).astype(jnp.bfloat16),
            "seq",
            -(offset + 1),
        ).astype(sent_key.dtype)
        came_key = came[..., :head_width]
        came_value = came[..., head_width:]
        extra_key = extra_key + came_key
        extra_value = extra_value + came_value
    own_key_grad = own_key_grad.at[row_count - rim_rows :].add(extra_key)
    own_value_grad = own_value_grad.at[row_count - rim_rows :].add(extra_value)
    block_out = jnp.swapaxes(state_output, 0, 1).astype(jnp.bfloat16)
    return (
        block_out,
        query_grad.astype(jnp.bfloat16),
        own_key_grad.astype(jnp.bfloat16),
        own_value_grad.astype(jnp.bfloat16),
        gain_grad,
        jnp.swapaxes(delta_grads[1], 0, 1).astype(jnp.bfloat16),
        jnp.swapaxes(delta_grads[2], 0, 1).astype(jnp.bfloat16),
        delta_grads[4].T,
        delta_grads[5].T,
    )


def solution(mesh):
    return jax.shard_map(
        body,
        mesh=mesh,
        in_specs=(
            P("seq", "head", None),
            P("seq", "head", None),
            P("seq", "head", None),
            P("head", None),
            P("seq", "head", None),
            P("seq", "head", None),
            P("seq", "head"),
            P("seq", "head"),
            P("seq", "head", None),
        ),
        out_specs=(
            P("seq", "head", None),
            P("seq", "head", None),
            P("seq", "head", None),
            P("seq", "head", None),
            P("head", None),
            P("seq", "head", None),
            P("seq", "head", None),
            P("seq", "head"),
            P("seq", "head"),
        ),
        check_vma=False,
    )
```
